256 devices in a mesh: row: 32 (over x, y, core), col: 8 (over z).
Axes of the slice: x: 4, y: 4, z: 8, core: 2. Of those that a mesh axis runs over, the one named last changes fastest.
Arguments:
- inputs: bfloat16 [1024, 16384], P('row', 'col'), may hold values from -6 to 6
- cotangent: bfloat16 [1024, 16384], P('row', 'col'), may hold values from -6 to 6
- gate_pre: bfloat16 [1024, 26624], P('col', 'row'), may hold values from -8 to 8
- up_pre: bfloat16 [1024, 26624], P('col', 'row'), may hold values from -6 to 6
- w_gate: bfloat16 [16384, 26624], P('col', 'row'), may hold values from -0.0390625 to 0.0390625
- w_up: bfloat16 [16384, 26624], P('col', 'row'), may hold values from -0.0390625 to 0.0390625
- w_down: bfloat16 [26624, 16384], P('row', 'col'), may hold values from -0.046875 to 0.046875
- up_a: bfloat16 [4, 16, 16384], P(None, None, 'col'), may hold values from -0.09375 to 0.09375
- up_b: bfloat16 [4, 16, 26624], P(None, None, 'row'), may hold values from -0.0390625 to 0.0390625
- down_a: bfloat16 [4, 16, 26624], P(None, None, 'row'), may hold values from -0.078125 to 0.078125
- down_b: bfloat16 [4, 16, 16384], P(None, None, 'col'), may hold values from -0.046875 to 0.046875
- tenant: int32 [1024], replicated, may hold values from 0 to 7, as said below
- adapter: int32 [8], replicated, may hold values from 0 to 3
Outputs:
- grad_inputs: bfloat16 [1024, 16384], P('row', 'col')
- grad_up_a: float32 [4, 16, 16384], P(None, None, 'col')
- up_second_gradient: float32 [4, 16, 26624], P(None, None, 'row')
- grad_down_a: float32 [4, 16, 26624], P(None, None, 'row')
- down_second_gradient: float32 [4, 16, 16384], P(None, None, 'col')
The draws below stay inside these ranges and needn't reach their ends.
Inputs may be any that keep to these rules, and one draw needn't show every extreme that they name: Tenant ids never fall from one token to the next and are constant on each aligned block of 128 tokens; the first token has tenant 0 and the last has tenant 8 - 1.
All inputs are finite; a program needn't handle non-finite values.
Results may differ from the reference program's by a relative error of at most 0.006.
Values may be sent and summed in bfloat16 or wider, within the bound.
No kernel may reach another device: no remote copies, remote signals or barrier semaphores. Data moves between devices by JAX's collectives and lax.ppermute only.
A program may use at most 128 MiB of HBM per device.

```python
import jax
import jax.numpy as jnp
from jax import lax

D = 16384
FF = 26624
RANK = 16
NADP = 4
NTEN = 8
BLOCK = 128
TOK = 1024
N_ROW = 32
N_COL = 8


def draw_tenant(key, part):
    blocks = TOK // BLOCK
    chosen = jnp.sort(jax.random.randint(key, (blocks,), 0, NTEN))
    places = jnp.arange(blocks)
    chosen = jnp.where(places == 0, 0, jnp.where(places == blocks - 1, NTEN - 1, chosen))
    return jnp.repeat(chosen, BLOCK).astype(jnp.int32)


def plant(array, stream_key, least, top_value):
    dims = array.shape
    place = [jax.random.randint(jax.random.fold_in(stream_key, axis), (), 0, dims[axis]) for axis in range(len(dims))]
    array = array.at[tuple(place)].set(least)
    longest = dims.index(max(dims))
    place[longest] = (place[longest] + 1) % dims[longest]
    return array.at[tuple(place)].set(top_value)


def block_levels(stream_key, shape, split, least, top_value):
    level, own = 1.0, jax.random.fold_in(stream_key, 6)
    for position, parts in split:
        draws = jnp.exp(jax.random.uniform(jax.random.fold_in(own, position), (parts,), jnp.float32, least / len(split), top_value / len(split)))
        level = level * jnp.repeat(draws, shape[position] // parts).reshape([-1 if axis == position else 1 for axis in range(len(shape))])
    return level


def bell_draw(stream_key, dims, deviation, bound, cuts=(), held_as=jnp.bfloat16):
    loudness = block_levels(stream_key, dims, cuts, -0.22, 0.18) if cuts else 1.0
    result = jax.random.normal(stream_key, dims, jnp.float32) * deviation * loudness
    return jnp.minimum(jnp.maximum(result, -bound), bound).astype(held_as)


def setup_inputs(seed: int = 0) -> dict:
    arg_keys = jax.random.split(jax.random.key(seed), 14)
    inputs = bell_draw(arg_keys[0], (TOK, D), 1.0, 6.0, ((0, 32), (1, 8)))
    cotangent = bell_draw(arg_keys[1], (TOK, D), 1.0, 6.0, ((0, 32), (1, 8)))
    gate_pre = bell_draw(arg_keys[2], (TOK, FF), 1.5, 8.0, ((0, 8), (1, 32)))
    up_pre = bell_draw(arg_keys[3], (TOK, FF), 1.0, 6.0, ((0, 8), (1, 32)))
    w_gate = bell_draw(arg_keys[4], (D, FF), FF ** -0.5, 0.0390625, ((0, 8), (1, 32)))
    w_up = bell_draw(arg_keys[5], (D, FF), FF ** -0.5, 0.0390625, ((0, 8), (1, 32)))
    w_down = bell_draw(arg_keys[6], (FF, D), D ** -0.5, 0.046875, ((0, 32), (1, 8)))
    up_a = bell_draw(arg_keys[7], (NADP, RANK, D), (D // 4) ** -0.5, 0.09375, ((2, 8),))
    up_b = bell_draw(arg_keys[8], (NADP, RANK, FF), FF ** -0.5, 0.0390625, ((2, 32),))
    down_a = bell_draw(arg_keys[9], (NADP, RANK, FF), (FF // 4) ** -0.5, 0.078125, ((2, 32),))
    down_b = bell_draw(arg_keys[10], (NADP, RANK, D), D ** -0.5, 0.046875, ((2, 8),))
    tenant = draw_tenant(jax.random.fold_in(arg_keys[13], 71), 0)
    adapter = plant(jax.random.randint(arg_keys[12], (NTEN,), 0, NADP), jax.random.fold_in(arg_keys[12], 1), 0, NADP - 1).astype(jnp.int32)
    return {"inputs": inputs, "cotangent": cotangent, "gate_pre": gate_pre, "up_pre": up_pre, "w_gate": w_gate, "w_up": w_up, "w_down": w_down, "up_a": up_a, "up_b": up_b, "down_a": down_a, "down_b": down_b, "tenant": tenant, "adapter": adapter}


ADAPTER_SCALING = 2.0


def rounded(value):
    return lax.optimization_barrier(value.astype(jnp.bfloat16)).astype(jnp.float32)


def hot_rows(tenant, adapter, n_adapt, rank_dim):
    ten_hot = (tenant[:, None] == jnp.arange(adapter.shape[0], dtype=jnp.int32)[None, :]).astype(jnp.float32)
    ada_hot = (adapter[:, None] == jnp.arange(n_adapt, dtype=jnp.int32)[None, :]).astype(jnp.float32)
    return jnp.repeat(jnp.dot(ten_hot, ada_hot), rank_dim, axis=1)


def reference(inputs, cotangent, gate_pre, up_pre, w_gate, w_up, w_down, up_a, up_b, down_a, down_b, tenant, adapter):
    adapter_rank_value = NADP * RANK
    up_a_all = up_a.reshape(adapter_rank_value, D)
    up_b_all = up_b.reshape(adapter_rank_value, FF)
    down_a_all = down_a.reshape(adapter_rank_value, FF)
    down_b_all = down_b.reshape(adapter_rank_value, D)
    active_tenant_mask = hot_rows(tenant, adapter, NADP, RANK)
    d_width = D // N_COL
    f_width = FF // N_ROW
    dh_base = jnp.dot(cotangent, w_down.T, preferred_element_type=jnp.float32)
    reduced_first_factor = jnp.zeros((TOK, 2 * adapter_rank_value), jnp.float32)
    for col_idx in range(N_COL):
        d_first = col_idx * d_width
        in_part = inputs[:, d_first:d_first + d_width]
        ct_part = cotangent[:, d_first:d_first + d_width]
        z_part = rounded(jnp.dot(in_part, up_a_all[:, d_first:d_first + d_width].T, preferred_element_type=jnp.float32))
        q_part = rounded(jnp.dot(ct_part, down_b_all[:, d_first:d_first + d_width].T, preferred_element_type=jnp.float32))
        reduced_first_factor = reduced_first_factor + jnp.concatenate([z_part, q_part], axis=1)
    up_adapter_output = (reduced_first_factor[:, :adapter_rank_value] * active_tenant_mask).astype(jnp.bfloat16)
    down_latent_rows = (ADAPTER_SCALING * reduced_first_factor[:, adapter_rank_value:] * active_tenant_mask).astype(jnp.bfloat16)
    d_hidden = dh_base + jnp.dot(down_latent_rows, down_a_all, preferred_element_type=jnp.float32)
    gate_f = gate_pre.astype(jnp.float32)
    up_f = up_pre.astype(jnp.float32)
    sigma = jax.nn.sigmoid(gate_f)
    silu_g = gate_f * sigma
    hidden = (silu_g * up_f).astype(jnp.bfloat16)
    up_gradient_rows = (d_hidden * silu_g).astype(jnp.bfloat16)
    d_gate = (d_hidden * up_f * sigma * (1.0 + gate_f * (1.0 - sigma))).astype(jnp.bfloat16)
    grad_down_a = jnp.dot(down_latent_rows.T, hidden, preferred_element_type=jnp.float32)
    up_second_gradient = ADAPTER_SCALING * jnp.dot(up_adapter_output.T, up_gradient_rows, preferred_element_type=jnp.float32)
    dx_base = jnp.dot(d_gate, w_gate.T, preferred_element_type=jnp.float32)
    dx_base = dx_base + jnp.dot(up_gradient_rows, w_up.T, preferred_element_type=jnp.float32)
    reduced_second_factor = jnp.zeros((TOK, 2 * adapter_rank_value), jnp.float32)
    for row_idx in range(N_ROW):
        f_first = row_idx * f_width
        up_part = up_gradient_rows[:, f_first:f_first + f_width]
        hid_part = hidden[:, f_first:f_first + f_width]
        z_part = rounded(jnp.dot(hid_part, down_a_all[:, f_first:f_first + f_width].T, preferred_element_type=jnp.float32))
        q_part = rounded(jnp.dot(up_part, up_b_all[:, f_first:f_first + f_width].T, preferred_element_type=jnp.float32))
        reduced_second_factor = reduced_second_factor + jnp.concatenate([z_part, q_part], axis=1)
    down_adapter_output = (reduced_second_factor[:, :adapter_rank_value] * active_tenant_mask).astype(jnp.bfloat16)
    up_latent_rows = (ADAPTER_SCALING * reduced_second_factor[:, adapter_rank_value:] * active_tenant_mask).astype(jnp.bfloat16)
    grad_inputs = (dx_base + jnp.dot(up_latent_rows, up_a_all, preferred_element_type=jnp.float32)).astype(jnp.bfloat16)
    grad_up_a = jnp.dot(up_latent_rows.T, inputs, preferred_element_type=jnp.float32)
    down_second_gradient = ADAPTER_SCALING * jnp.dot(down_adapter_output.T, cotangent, preferred_element_type=jnp.float32)
    return (grad_inputs, grad_up_a.reshape(NADP, RANK, D), up_second_gradient.reshape(NADP, RANK, FF),
            grad_down_a.reshape(NADP, RANK, FF), down_second_gradient.reshape(NADP, RANK, D))
```

```python
import jax
import jax.numpy as jnp
from jax import lax
from jax.sharding import PartitionSpec as P

ADAPTER_SCALING = 2.0


def hot_rows(tenant, adapter, first_tok, tok_count, n_adapt, rank_dim):
    tok_ids = lax.dynamic_slice_in_dim(tenant, first_tok, tok_count)
    ten_hot = (tok_ids[:, None] == jnp.arange(adapter.shape[0], dtype=jnp.int32)[None, :]).astype(
        jnp.float32
    )
    ada_hot = (adapter[:, None] == jnp.arange(n_adapt, dtype=jnp.int32)[None, :]).astype(
        jnp.float32
    )
    return jnp.repeat(jnp.dot(ten_hot, ada_hot), rank_dim, axis=1)


def on_device(
    inputs,
    cotangent,
    gate_pre,
    up_pre,
    w_gate,
    w_up,
    w_down,
    up_a,
    up_b,
    down_a,
    down_b,
    tenant,
    adapter,
):
    n_adapt, rank_dim, d_width = up_a.shape
    f_width = up_b.shape[2]
    arv = n_adapt * rank_dim
    tok_row = inputs.shape[0]
    tok_all = tenant.shape[0]
    tok_col = tok_all // lax.axis_size("col")
    up_a_all = up_a.reshape(arv, d_width)
    up_b_all = up_b.reshape(arv, f_width)
    down_a_all = down_a.reshape(arv, f_width)
    down_b_all = down_b.reshape(arv, d_width)
    token_row_mask = hot_rows(
        tenant, adapter, lax.axis_index("row") * tok_row, tok_row, n_adapt, rank_dim
    )
    z_part = jnp.dot(inputs, up_a_all.T, preferred_element_type=jnp.float32)
    q_part = jnp.dot(cotangent, down_b_all.T, preferred_element_type=jnp.float32)
    narrow_own = jnp.concatenate([z_part, q_part], axis=1).astype(jnp.bfloat16)
    packed_1 = jnp.concatenate([cotangent, inputs, narrow_own], axis=1)
    gathered_1 = lax.all_gather(packed_1, "row", axis=0, tiled=True)
    ct_column = gathered_1[:, :d_width]
    in_column = gathered_1[:, d_width : 2 * d_width]
    narrow_column = gathered_1[:, 2 * d_width :]
    dh_term = jnp.dot(ct_column, w_down.T, preferred_element_type=jnp.float32)
    summed_1 = lax.psum_scatter(
        jnp.concatenate([dh_term, narrow_column.astype(jnp.float32)], axis=1),
        "col",
        scatter_dimension=0,
        tiled=True,
    )
    dh_base = summed_1[:, :f_width]
    reduced_first_factor = summed_1[:, f_width:]
    active_tenant_mask = hot_rows(
        tenant, adapter, lax.axis_index("col") * tok_col, tok_col, n_adapt, rank_dim
    )
    up_adapter_output = (reduced_first_factor[:, :arv] * active_tenant_mask).astype(jnp.bfloat16)
    down_latent_rows = (
        ADAPTER_SCALING * reduced_first_factor[:, arv:] * active_tenant_mask
    ).astype(jnp.bfloat16)
    d_hidden = dh_base + jnp.dot(down_latent_rows, down_a_all, preferred_element_type=jnp.float32)
    gate_f = gate_pre.astype(jnp.float32)
    up_f = up_pre.astype(jnp.float32)
    sigma = jax.nn.sigmoid(gate_f)
    silu_g = gate_f * sigma
    hidden = (silu_g * up_f).astype(jnp.bfloat16)
    up_gradient_rows = (d_hidden * silu_g).astype(jnp.bfloat16)
    d_gate = (d_hidden * up_f * sigma * (1.0 + gate_f * (1.0 - sigma))).astype(jnp.bfloat16)
    grad_down_a = jnp.dot(down_latent_rows.T, hidden, preferred_element_type=jnp.float32)
    up_second_gradient = ADAPTER_SCALING * jnp.dot(
        up_adapter_output.T, up_gradient_rows, preferred_element_type=jnp.float32
    )
    z_hidden = jnp.dot(hidden, down_a_all.T, preferred_element_type=jnp.float32).astype(
        jnp.bfloat16
    )
    q_hidden = jnp.dot(up_gradient_rows, up_b_all.T, preferred_element_type=jnp.float32).astype(
        jnp.bfloat16
    )
    gathered_2 = lax.all_gather(
        jnp.concatenate([d_gate, up_gradient_rows, z_hidden, q_hidden], axis=1),
        "col",
        axis=0,
        tiled=True,
    )
    grad_down_a, up_second_gradient = lax.psum((grad_down_a, up_second_gradient), "col")
    gate_rows = gathered_2[:, :f_width]
    up_rows = gathered_2[:, f_width : 2 * f_width]
    narrow_rows = gathered_2[:, 2 * f_width :].astype(jnp.float32)
    dx_term = jnp.dot(gate_rows, w_gate.T, preferred_element_type=jnp.float32)
    dx_term = dx_term + jnp.dot(up_rows, w_up.T, preferred_element_type=jnp.float32)
    summed_2 = lax.psum_scatter(
        jnp.concatenate([dx_term, narrow_rows], axis=1), "row", scatter_dimension=0, tiled=True
    )
    dx_base = summed_2[:, :d_width]
    reduced_second_factor = summed_2[:, d_width:]
    down_adapter_output = (reduced_second_factor[:, :arv] * token_row_mask).astype(jnp.bfloat16)
    up_latent_rows = (
        ADAPTER_SCALING * reduced_second_factor[:, arv:] * token_row_mask
    ).astype(jnp.bfloat16)
    grad_inputs = (
        dx_base + jnp.dot(up_latent_rows, up_a_all, preferred_element_type=jnp.float32)
    ).astype(jnp.bfloat16)
    latent_all = lax.all_gather(
        jnp.concatenate([down_adapter_output, up_latent_rows], axis=1), "row", axis=0, tiled=True
    )
    grad_up_a = jnp.dot(latent_all[:, arv:].T, in_column, preferred_element_type=jnp.float32)
    down_second_gradient = ADAPTER_SCALING * jnp.dot(
        latent_all[:, :arv].T, ct_column, preferred_element_type=jnp.float32
    )
    return (
        grad_inputs,
        grad_up_a.reshape(n_adapt, rank_dim, d_width),
        up_second_gradient.reshape(n_adapt, rank_dim, f_width),
        grad_down_a.reshape(n_adapt, rank_dim, f_width),
        down_second_gradient.reshape(n_adapt, rank_dim, d_width),
    )


def solution(mesh):
    return jax.shard_map(
        on_device,
        mesh=mesh,
        in_specs=(
            P("row", "col"),
            P("row", "col"),
            P("col", "row"),
            P("col", "row"),
            P("col", "row"),
            P("col", "row"),
            P("row", "col"),
            P(None, None, "col"),
            P(None, None, "row"),
            P(None, None, "row"),
            P(None, None, "col"),
            P(),
            P(),
        ),
        out_specs=(
            P("row", "col"),
            P(None, None, "col"),
            P(None, None, "row"),
            P(None, None, "row"),
            P(None, None, "col"),
        ),
        check_vma=False,
    )
```

```python
import jax
import jax.numpy as jnp
from jax import lax
from jax.sharding import PartitionSpec as P

ADAPTER_SCALING = 2.0


def hot_rows(tenant, adapter, first_tok, tok_count, n_adapt, rank_dim):
    tok_ids = lax.dynamic_slice_in_dim(tenant, first_tok, tok_count)
    ten_hot = (tok_ids[:, None] == jnp.arange(adapter.shape[0], dtype=jnp.int32)[None, :]).astype(
        jnp.float32
    )
    ada_hot = (adapter[:, None] == jnp.arange(n_adapt, dtype=jnp.int32)[None, :]).astype(
        jnp.float32
    )
    return jnp.repeat(jnp.dot(ten_hot, ada_hot), rank_dim, axis=1)


def on_device(
    inputs,
    cotangent,
    gate_pre,
    up_pre,
    w_gate,
    w_up,
    w_down,
    up_a,
    up_b,
    down_a,
    down_b,
    tenant,
    adapter,
):
    n_adapt, rank_dim, d_width = up_a.shape
    f_width = up_b.shape[2]
    arv = n_adapt * rank_dim
    tok_row = inputs.shape[0]
    tok_all = tenant.shape[0]
    tok_col = tok_all // lax.axis_size("col")
    up_a_all = up_a.reshape(arv, d_width)
    up_b_all = up_b.reshape(arv, f_width)
    down_a_all = down_a.reshape(arv, f_width)
    down_b_all = down_b.reshape(arv, d_width)
    token_row_mask = hot_rows(
        tenant, adapter, lax.axis_index("row") * tok_row, tok_row, n_adapt, rank_dim
    )
    z_part = jnp.dot(inputs, up_a_all.T, preferred_element_type=jnp.float32)
    q_part = jnp.dot(cotangent, down_b_all.T, preferred_element_type=jnp.float32)
    narrow_own = jnp.concatenate([z_part, q_part], axis=1).astype(jnp.bfloat16)
    packed_1 = jnp.concatenate([cotangent, inputs, narrow_own], axis=1)
    gathered_1 = lax.all_gather(packed_1, "row", axis=0, tiled=True)
    ct_column = gathered_1[:, :d_width]
    in_column = gathered_1[:, d_width : 2 * d_width]
    narrow_column = gathered_1[:, 2 * d_width :]
    dh_term = jnp.dot(ct_column, w_down.T, preferred_element_type=jnp.float32)
    summed_1 = lax.psum_scatter(
        jnp.concatenate([dh_term, narrow_column.astype(jnp.float32)], axis=1),
        "col",
        scatter_dimension=0,
        tiled=True,
    )
    dh_base = summed_1[:, :f_width]
    reduced_first_factor = summed_1[:, f_width:]
    active_tenant_mask = hot_rows(
        tenant, adapter, lax.axis_index("col") * tok_col, tok_col, n_adapt, rank_dim
    )
    up_adapter_output = (reduced_first_factor[:, :arv] * active_tenant_mask).astype(jnp.bfloat16)
    down_latent_rows = (
        ADAPTER_SCALING * reduced_first_factor[:, arv:] * active_tenant_mask
    ).astype(jnp.bfloat16)
    d_hidden = dh_base + jnp.dot(down_latent_rows, down_a_all, preferred_element_type=jnp.float32)
    gate_f = gate_pre.astype(jnp.float32)
    up_f = up_pre.astype(jnp.float32)
    sigma = jax.nn.sigmoid(gate_f)
    silu_g = gate_f * sigma
    hidden = (silu_g * up_f).astype(jnp.bfloat16)
    up_gradient_rows = (d_hidden * silu_g).astype(jnp.bfloat16)
    d_gate = (d_hidden * up_f * sigma * (1.0 + gate_f * (1.0 - sigma))).astype(jnp.bfloat16)
    z_hidden = jnp.dot(hidden, down_a_all.T, preferred_element_type=jnp.float32).astype(
        jnp.bfloat16
    )
    q_hidden = jnp.dot(up_gradient_rows, up_b_all.T, preferred_element_type=jnp.float32).astype(
        jnp.bfloat16
    )
    gathered_2 = lax.all_gather(
        jnp.concatenate(
            [
                d_gate,
                up_gradient_rows,
                hidden,
                z_hidden,
                q_hidden,
                up_adapter_output,
                down_latent_rows,
            ],
            axis=1,
        ),
        "col",
        axis=0,
        tiled=True,
    )
    hidden_rows = gathered_2[:, 2 * f_width : 3 * f_width]
    adapter_rows = gathered_2[:, 3 * f_width + 2 * arv :]
    grad_down_a = jnp.dot(
        adapter_rows[:, arv:].T, hidden_rows, preferred_element_type=jnp.float32
    )
    gate_rows = gathered_2[:, :f_width]
    up_rows = gathered_2[:, f_width : 2 * f_width]
    up_second_gradient = ADAPTER_SCALING * jnp.dot(
        adapter_rows[:, :arv].T, up_rows, preferred_element_type=jnp.float32
    )
    narrow_rows = gathered_2[:, 3 * f_width : 3 * f_width + 2 * arv].astype(jnp.float32)
    dx_term = jnp.dot(gate_rows, w_gate.T, preferred_element_type=jnp.float32)
    dx_term = dx_term + jnp.dot(up_rows, w_up.T, preferred_element_type=jnp.float32)
    summed_2 = lax.psum_scatter(
        jnp.concatenate([dx_term, narrow_rows], axis=1), "row", scatter_dimension=0, tiled=True
    )
    dx_base = summed_2[:, :d_width]
    reduced_second_factor = summed_2[:, d_width:]
    down_adapter_output = (reduced_second_factor[:, :arv] * token_row_mask).astype(jnp.bfloat16)
    up_latent_rows = (
        ADAPTER_SCALING * reduced_second_factor[:, arv:] * token_row_mask
    ).astype(jnp.bfloat16)
    grad_inputs = (
        dx_base + jnp.dot(up_latent_rows, up_a_all, preferred_element_type=jnp.float32)
    ).astype(jnp.bfloat16)
    latent_all = lax.all_gather(
        jnp.concatenate([down_adapter_output, up_latent_rows], axis=1), "row", axis=0, tiled=True
    )
    grad_up_a = jnp.dot(latent_all[:, arv:].T, in_column, preferred_element_type=jnp.float32)
    down_second_gradient = ADAPTER_SCALING * jnp.dot(
        latent_all[:, :arv].T, ct_column, preferred_element_type=jnp.float32
    )
    return (
        grad_inputs,
        grad_up_a.reshape(n_adapt, rank_dim, d_width),
        up_second_gradient.reshape(n_adapt, rank_dim, f_width),
        grad_down_a.reshape(n_adapt, rank_dim, f_width),
        down_second_gradient.reshape(n_adapt, rank_dim, d_width),
    )


def solution(mesh):
    return jax.shard_map(
        on_device,
        mesh=mesh,
        in_specs=(
            P("row", "col"),
            P("row", "col"),
            P("col", "row"),
            P("col", "row"),
            P("col", "row"),
            P("col", "row"),
            P("row", "col"),
            P(None, None, "col"),
            P(None, None, "row"),
            P(None, None, "row"),
            P(None, None, "col"),
            P(),
            P(),
        ),
        out_specs=(
            P("row", "col"),
            P(None, None, "col"),
            P(None, None, "row"),
            P(None, None, "row"),
            P(None, None, "col"),
        ),
        check_vma=False,
    )
```

```python
import jax
import jax.numpy as jnp
from jax import lax
from jax.sharding import PartitionSpec as P

ADAPTER_SCALING = 2.0


def hot_rows(tenant, adapter, first_tok, tok_count, n_adapt, rank_dim):
    tok_ids = lax.dynamic_slice_in_dim(tenant, first_tok, tok_count)
    ten_hot = (tok_ids[:, None] == jnp.arange(adapter.shape[0], dtype=jnp.int32)[None, :]).astype(
        jnp.float32
    )
    ada_hot = (adapter[:, None] == jnp.arange(n_adapt, dtype=jnp.int32)[None, :]).astype(
        jnp.float32
    )
    return jnp.repeat(jnp.dot(ten_hot, ada_hot), rank_dim, axis=1)


def on_device(
    inputs,
    cotangent,
    gate_pre,
    up_pre,
    w_gate,
    w_up,
    w_down,
    up_a,
    up_b,
    down_a,
    down_b,
    tenant,
    adapter,
):
    n_adapt, rank_dim, d_width = up_a.shape
    f_width = up_b.shape[2]
    arv = n_adapt * rank_dim
    tok_row = inputs.shape[0]
    tok_all = tenant.shape[0]
    tok_col = tok_all // lax.axis_size("col")
    up_a_all = up_a.reshape(arv, d_width)
    up_b_all = up_b.reshape(arv, f_width)
    down_a_all = down_a.reshape(arv, f_width)
    down_b_all = down_b.reshape(arv, d_width)
    token_row_mask = hot_rows(
        tenant, adapter, lax.axis_index("row") * tok_row, tok_row, n_adapt, rank_dim
    )
    z_part = jnp.dot(inputs, up_a_all.T, preferred_element_type=jnp.float32)
    q_part = jnp.dot(cotangent, down_b_all.T, preferred_element_type=jnp.float32)
    narrow_own = jnp.concatenate([z_part, q_part], axis=1).astype(jnp.bfloat16)
    packed_1 = jnp.concatenate([cotangent, inputs, narrow_own], axis=1)
    gathered_1 = lax.all_gather(packed_1, "row", axis=0, tiled=True)
    ct_column = gathered_1[:, :d_width]
    in_column = gathered_1[:, d_width : 2 * d_width]
    narrow_column = gathered_1[:, 2 * d_width :]
    dh_term = jnp.dot(ct_column, w_down.T, preferred_element_type=jnp.float32)
    summed_1 = lax.psum_scatter(
        jnp.concatenate([dh_term, narrow_column.astype(jnp.float32)], axis=1),
        "col",
        scatter_dimension=0,
        tiled=True,
    )
    dh_base = summed_1[:, :f_width]
    reduced_first_factor = summed_1[:, f_width:]
    active_tenant_mask = hot_rows(
        tenant, adapter, lax.axis_index("col") * tok_col, tok_col, n_adapt, rank_dim
    )
    up_adapter_output = (reduced_first_factor[:, :arv] * active_tenant_mask).astype(jnp.bfloat16)
    down_latent_rows = (
        ADAPTER_SCALING * reduced_first_factor[:, arv:] * active_tenant_mask
    ).astype(jnp.bfloat16)
    d_hidden = dh_base + jnp.dot(down_latent_rows, down_a_all, preferred_element_type=jnp.float32)
    gate_f = gate_pre.astype(jnp.float32)
    up_f = up_pre.astype(jnp.float32)
    sigma = jax.nn.sigmoid(gate_f)
    silu_g = gate_f * sigma
    hidden = (silu_g * up_f).astype(jnp.bfloat16)
    up_gradient_rows = (d_hidden * silu_g).astype(jnp.bfloat16)
    d_gate = (d_hidden * up_f * sigma * (1.0 + gate_f * (1.0 - sigma))).astype(jnp.bfloat16)
    z_hidden = jnp.dot(hidden, down_a_all.T, preferred_element_type=jnp.float32).astype(
        jnp.bfloat16
    )
    q_hidden = jnp.dot(up_gradient_rows, up_b_all.T, preferred_element_type=jnp.float32).astype(
        jnp.bfloat16
    )
    gathered_2 = lax.all_gather(
        jnp.concatenate(
            [
                d_gate,
                up_gradient_rows,
                hidden,
                z_hidden,
                q_hidden,
                up_adapter_output,
                down_latent_rows,
            ],
            axis=1,
        ),
        "col",
        axis=0,
        tiled=True,
    )
    hidden_rows = gathered_2[:, 2 * f_width : 3 * f_width]
    adapter_rows = gathered_2[:, 3 * f_width + 2 * arv :]
    grad_down_a = jnp.dot(
        adapter_rows[:, arv:].T, hidden_rows, preferred_element_type=jnp.float32
    )
    gate_rows = gathered_2[:, :f_width]
    up_rows = gathered_2[:, f_width : 2 * f_width]
    up_second_gradient = ADAPTER_SCALING * jnp.dot(
        adapter_rows[:, :arv].T, up_rows, preferred_element_type=jnp.float32
    )
    narrow_rows = gathered_2[:, 3 * f_width : 3 * f_width + 2 * arv].astype(jnp.float32)
    dx_term = jnp.dot(gate_rows, w_gate.T, preferred_element_type=jnp.float32)
    dx_term = dx_term + jnp.dot(up_rows, w_up.T, preferred_element_type=jnp.float32)
    packed_2 = jnp.concatenate([dx_term, narrow_rows], axis=1).astype(jnp.bfloat16)
    n_row = lax.axis_size("row")
    swapped_2 = lax.all_to_all(packed_2, "row", 0, 0, tiled=True)
    summed_2 = swapped_2.reshape(n_row, tok_row, packed_2.shape[1]).astype(jnp.float32).sum(0)
    dx_base = summed_2[:, :d_width]
    reduced_second_factor = summed_2[:, d_width:]
    down_adapter_output = (reduced_second_factor[:, :arv] * token_row_mask).astype(jnp.bfloat16)
    up_latent_rows = (
        ADAPTER_SCALING * reduced_second_factor[:, arv:] * token_row_mask
    ).astype(jnp.bfloat16)
    grad_inputs = (
        dx_base + jnp.dot(up_latent_rows, up_a_all, preferred_element_type=jnp.float32)
    ).astype(jnp.bfloat16)
    latent_own = jnp.concatenate([down_adapter_output, up_latent_rows], axis=1)
    latent_all = lax.all_to_all(jnp.tile(latent_own, (n_row, 1)), "row", 0, 0, tiled=True)
    grad_up_a = jnp.dot(latent_all[:, arv:].T, in_column, preferred_element_type=jnp.float32)
    down_second_gradient = ADAPTER_SCALING * jnp.dot(
        latent_all[:, :arv].T, ct_column, preferred_element_type=jnp.float32
    )
    return (
        grad_inputs,
        grad_up_a.reshape(n_adapt, rank_dim, d_width),
        up_second_gradient.reshape(n_adapt, rank_dim, f_width),
        grad_down_a.reshape(n_adapt, rank_dim, f_width),
        down_second_gradient.reshape(n_adapt, rank_dim, d_width),
    )


def solution(mesh):
    return jax.shard_map(
        on_device,
        mesh=mesh,
        in_specs=(
            P("row", "col"),
            P("row", "col"),
            P("col", "row"),
            P("col", "row"),
            P("col", "row"),
            P("col", "row"),
            P("row", "col"),
            P(None, None, "col"),
            P(None, None, "row"),
            P(None, None, "row"),
            P(None, None, "col"),
            P(),
            P(),
        ),
        out_specs=(
            P("row", "col"),
            P(None, None, "col"),
            P(None, None, "row"),
            P(None, None, "row"),
            P(None, None, "col"),
        ),
        check_vma=False,
    )
```

```python
import jax
import jax.numpy as jnp
from jax import lax
from jax.sharding import PartitionSpec as P

ADAPTER_SCALING = 2.0


def hot_rows(tenant, adapter, first_tok, tok_count, n_adapt, rank_dim):
    tok_ids = lax.dynamic_slice_in_dim(tenant, first_tok, tok_count)
    ten_hot = (tok_ids[:, None] == jnp.arange(adapter.shape[0], dtype=jnp.int32)[None, :]).astype(
        jnp.float32
    )
    ada_hot = (adapter[:, None] == jnp.arange(n_adapt, dtype=jnp.int32)[None, :]).astype(
        jnp.float32
    )
    return jnp.repeat(jnp.dot(ten_hot, ada_hot), rank_dim, axis=1)


def on_device(
    inputs,
    cotangent,
    gate_pre,
    up_pre,
    w_gate,
    w_up,
    w_down,
    up_a,
    up_b,
    down_a,
    down_b,
    tenant,
    adapter,
):
    n_adapt, rank_dim, d_width = up_a.shape
    f_width = up_b.shape[2]
    arv = n_adapt * rank_dim
    tok_row = inputs.shape[0]
    tok_all = tenant.shape[0]
    tok_col = tok_all // lax.axis_size("col")
    up_a_all = up_a.reshape(arv, d_width)
    up_b_all = up_b.reshape(arv, f_width)
    down_a_all = down_a.reshape(arv, f_width)
    down_b_all = down_b.reshape(arv, d_width)
    token_row_mask = hot_rows(
        tenant, adapter, lax.axis_index("row") * tok_row, tok_row, n_adapt, rank_dim
    )
    z_part = jnp.dot(inputs, up_a_all.T, preferred_element_type=jnp.float32)
    q_part = jnp.dot(cotangent, down_b_all.T, preferred_element_type=jnp.float32)
    narrow_own = jnp.concatenate([z_part, q_part], axis=1).astype(jnp.bfloat16)
    packed_1 = jnp.concatenate([cotangent, inputs, narrow_own], axis=1)
    gathered_1 = lax.all_gather(packed_1, "row", axis=0, tiled=True)
    ct_column = gathered_1[:, :d_width]
    in_column = gathered_1[:, d_width : 2 * d_width]
    narrow_column = gathered_1[:, 2 * d_width :]
    dh_term = jnp.dot(ct_column, w_down.T, preferred_element_type=jnp.float32)
    summed_1 = lax.psum_scatter(
        jnp.concatenate([dh_term, narrow_column.astype(jnp.float32)], axis=1),
        "col",
        scatter_dimension=0,
        tiled=True,
    )
    dh_base = summed_1[:, :f_width]
    reduced_first_factor = summed_1[:, f_width:]
    active_tenant_mask = hot_rows(
        tenant, adapter, lax.axis_index("col") * tok_col, tok_col, n_adapt, rank_dim
    )
    up_adapter_output = (reduced_first_factor[:, :arv] * active_tenant_mask).astype(jnp.bfloat16)
    down_latent_rows = (
        ADAPTER_SCALING * reduced_first_factor[:, arv:] * active_tenant_mask
    ).astype(jnp.bfloat16)
    d_hidden = dh_base + jnp.dot(down_latent_rows, down_a_all, preferred_element_type=jnp.float32)
    gate_f = gate_pre.astype(jnp.float32)
    up_f = up_pre.astype(jnp.float32)
    sigma = jax.nn.sigmoid(gate_f)
    silu_g = gate_f * sigma
    hidden = (silu_g * up_f).astype(jnp.bfloat16)
    up_gradient_rows = (d_hidden * silu_g).astype(jnp.bfloat16)
    d_gate = (d_hidden * up_f * sigma * (1.0 + gate_f * (1.0 - sigma))).astype(jnp.bfloat16)
    z_hidden = jnp.dot(hidden, down_a_all.T, preferred_element_type=jnp.float32).astype(
        jnp.bfloat16
    )
    q_hidden = jnp.dot(up_gradient_rows, up_b_all.T, preferred_element_type=jnp.float32).astype(
        jnp.bfloat16
    )
    grad_down_a = jnp.dot(down_latent_rows.T, hidden, preferred_element_type=jnp.float32)
    up_second_gradient = ADAPTER_SCALING * jnp.dot(
        up_adapter_output.T, up_gradient_rows, preferred_element_type=jnp.float32
    )
    gathered_2 = lax.all_gather(
        jnp.concatenate([d_gate, up_gradient_rows, z_hidden, q_hidden], axis=1),
        "col",
        axis=0,
        tiled=True,
    )
    (grad_down_a, up_second_gradient), gathered_2 = lax.optimization_barrier(
        ((grad_down_a, up_second_gradient), gathered_2)
    )
    grad_down_a, up_second_gradient = lax.psum((grad_down_a, up_second_gradient), "col")
    gate_rows = gathered_2[:, :f_width]
    up_rows = gathered_2[:, f_width : 2 * f_width]
    narrow_rows = gathered_2[:, 2 * f_width :].astype(jnp.float32)
    dx_term = jnp.dot(gate_rows, w_gate.T, preferred_element_type=jnp.float32)
    dx_term = dx_term + jnp.dot(up_rows, w_up.T, preferred_element_type=jnp.float32)
    packed_2 = jnp.concatenate([dx_term, narrow_rows], axis=1).astype(jnp.bfloat16)
    n_row = lax.axis_size("row")
    swapped_2 = lax.all_to_all(packed_2, "row", 0, 0, tiled=True)
    summed_2 = swapped_2.reshape(n_row, tok_row, packed_2.shape[1]).astype(jnp.float32).sum(0)
    dx_base = summed_2[:, :d_width]
    reduced_second_factor = summed_2[:, d_width:]
    down_adapter_output = (reduced_second_factor[:, :arv] * token_row_mask).astype(jnp.bfloat16)
    up_latent_rows = (
        ADAPTER_SCALING * reduced_second_factor[:, arv:] * token_row_mask
    ).astype(jnp.bfloat16)
    grad_inputs = (
        dx_base + jnp.dot(up_latent_rows, up_a_all, preferred_element_type=jnp.float32)
    ).astype(jnp.bfloat16)
    latent_own = jnp.concatenate([down_adapter_output, up_latent_rows], axis=1)
    latent_all = lax.all_to_all(jnp.tile(latent_own, (n_row, 1)), "row", 0, 0, tiled=True)
    grad_up_a = jnp.dot(latent_all[:, arv:].T, in_column, preferred_element_type=jnp.float32)
    down_second_gradient = ADAPTER_SCALING * jnp.dot(
        latent_all[:, :arv].T, ct_column, preferred_element_type=jnp.float32
    )
    return (
        grad_inputs,
        grad_up_a.reshape(n_adapt, rank_dim, d_width),
        up_second_gradient.reshape(n_adapt, rank_dim, f_width),
        grad_down_a.reshape(n_adapt, rank_dim, f_width),
        down_second_gradient.reshape(n_adapt, rank_dim, d_width),
    )


def solution(mesh):
    return jax.shard_map(
        on_device,
        mesh=mesh,
        in_specs=(
            P("row", "col"),
            P("row", "col"),
            P("col", "row"),
            P("col", "row"),
            P("col", "row"),
            P("col", "row"),
            P("row", "col"),
            P(None, None, "col"),
            P(None, None, "row"),
            P(None, None, "row"),
            P(None, None, "col"),
            P(),
            P(),
        ),
        out_specs=(
            P("row", "col"),
            P(None, None, "col"),
            P(None, None, "row"),
            P(None, None, "row"),
            P(None, None, "col"),
        ),
        check_vma=False,
    )
```

```python
import jax
import jax.numpy as jnp
from jax import lax
from jax.sharding import PartitionSpec as P

ADAPTER_SCALING = 2.0


def hot_rows(tenant, adapter, first_tok, tok_count, n_adapt, rank_dim):
    tok_ids = lax.dynamic_slice_in_dim(tenant, first_tok, tok_count)
    ten_hot = (tok_ids[:, None] == jnp.arange(adapter.shape[0], dtype=jnp.int32)[None, :]).astype(
        jnp.float32
    )
    ada_hot = (adapter[:, None] == jnp.arange(n_adapt, dtype=jnp.int32)[None, :]).astype(
        jnp.float32
    )
    return jnp.repeat(jnp.dot(ten_hot, ada_hot), rank_dim, axis=1)


def on_device(
    inputs,
    cotangent,
    gate_pre,
    up_pre,
    w_gate,
    w_up,
    w_down,
    up_a,
    up_b,
    down_a,
    down_b,
    tenant,
    adapter,
):
    n_adapt, rank_dim, d_width = up_a.shape
    f_width = up_b.shape[2]
    arv = n_adapt * rank_dim
    tok_row = inputs.shape[0]
    tok_all = tenant.shape[0]
    tok_col = tok_all // lax.axis_size("col")
    up_a_all = up_a.reshape(arv, d_width)
    up_b_all = up_b.reshape(arv, f_width)
    down_a_all = down_a.reshape(arv, f_width)
    down_b_all = down_b.reshape(arv, d_width)
    token_row_mask = hot_rows(
        tenant, adapter, lax.axis_index("row") * tok_row, tok_row, n_adapt, rank_dim
    )
    z_part = jnp.dot(inputs, up_a_all.T, preferred_element_type=jnp.float32)
    q_part = jnp.dot(cotangent, down_b_all.T, preferred_element_type=jnp.float32)
    narrow_own = jnp.concatenate([z_part, q_part], axis=1).astype(jnp.bfloat16)
    packed_1 = jnp.concatenate([cotangent, inputs, narrow_own], axis=1)
    gathered_1 = lax.all_gather(packed_1, "row", axis=0, tiled=True)
    ct_column = gathered_1[:, :d_width]
    in_column = gathered_1[:, d_width : 2 * d_width]
    narrow_column = gathered_1[:, 2 * d_width :]
    dh_term = jnp.dot(ct_column, w_down.T, preferred_element_type=jnp.float32)
    summed_1 = lax.psum_scatter(
        jnp.concatenate([dh_term, narrow_column.astype(jnp.float32)], axis=1),
        "col",
        scatter_dimension=0,
        tiled=True,
    )
    dh_base = summed_1[:, :f_width]
    reduced_first_factor = summed_1[:, f_width:]
    active_tenant_mask = hot_rows(
        tenant, adapter, lax.axis_index("col") * tok_col, tok_col, n_adapt, rank_dim
    )
    up_adapter_output = (reduced_first_factor[:, :arv] * active_tenant_mask).astype(jnp.bfloat16)
    down_latent_rows = (
        ADAPTER_SCALING * reduced_first_factor[:, arv:] * active_tenant_mask
    ).astype(jnp.bfloat16)
    d_hidden = dh_base + jnp.dot(down_latent_rows, down_a_all, preferred_element_type=jnp.float32)
    gate_f = gate_pre.astype(jnp.float32)
    up_f = up_pre.astype(jnp.float32)
    sigma = jax.nn.sigmoid(gate_f)
    silu_g = gate_f * sigma
    hidden = (silu_g * up_f).astype(jnp.bfloat16)
    up_gradient_rows = (d_hidden * silu_g).astype(jnp.bfloat16)
    d_gate = (d_hidden * up_f * sigma * (1.0 + gate_f * (1.0 - sigma))).astype(jnp.bfloat16)
    z_hidden = jnp.dot(hidden, down_a_all.T, preferred_element_type=jnp.float32).astype(
        jnp.bfloat16
    )
    q_hidden = jnp.dot(up_gradient_rows, up_b_all.T, preferred_element_type=jnp.float32).astype(
        jnp.bfloat16
    )
    grad_down_a = jnp.dot(down_latent_rows.T, hidden, preferred_element_type=jnp.float32)
    up_second_gradient = ADAPTER_SCALING * jnp.dot(
        up_adapter_output.T, up_gradient_rows, preferred_element_type=jnp.float32
    )
    gathered_2 = lax.all_gather(
        jnp.concatenate([d_gate, up_gradient_rows, z_hidden, q_hidden], axis=1),
        "col",
        axis=0,
        tiled=True,
    )
    (grad_down_a, up_second_gradient), gathered_2 = lax.optimization_barrier(
        ((grad_down_a, up_second_gradient), gathered_2)
    )
    grad_down_a, up_second_gradient = lax.psum((grad_down_a, up_second_gradient), "col")
    gate_rows = gathered_2[:, :f_width]
    up_rows = gathered_2[:, f_width : 2 * f_width]
    n_row = lax.axis_size("row")
    swapped_n = lax.all_to_all(gathered_2[:, 2 * f_width :], "row", 0, 0, tiled=True)
    reduced_second_factor = (
        swapped_n.reshape(n_row, tok_row, 2 * arv).astype(jnp.float32).sum(0)
    )
    down_adapter_output = (reduced_second_factor[:, :arv] * token_row_mask).astype(jnp.bfloat16)
    up_latent_rows = (
        ADAPTER_SCALING * reduced_second_factor[:, arv:] * token_row_mask
    ).astype(jnp.bfloat16)
    latent_own = jnp.concatenate([down_adapter_output, up_latent_rows], axis=1)
    latent_all = lax.all_to_all(jnp.tile(latent_own, (n_row, 1)), "row", 0, 0, tiled=True)
    grad_up_a = jnp.dot(latent_all[:, arv:].T, in_column, preferred_element_type=jnp.float32)
    down_second_gradient = ADAPTER_SCALING * jnp.dot(
        latent_all[:, :arv].T, ct_column, preferred_element_type=jnp.float32
    )
    dx_term = jnp.dot(gate_rows, w_gate.T, preferred_element_type=jnp.float32)
    dx_term = dx_term + jnp.dot(up_rows, w_up.T, preferred_element_type=jnp.float32)
    swapped_2 = lax.all_to_all(dx_term.astype(jnp.bfloat16), "row", 0, 0, tiled=True)
    dx_base = swapped_2.reshape(n_row, tok_row, d_width).astype(jnp.float32).sum(0)
    grad_inputs = (
        dx_base + jnp.dot(up_latent_rows, up_a_all, preferred_element_type=jnp.float32)
    ).astype(jnp.bfloat16)
    return (
        grad_inputs,
        grad_up_a.reshape(n_adapt, rank_dim, d_width),
        up_second_gradient.reshape(n_adapt, rank_dim, f_width),
        grad_down_a.reshape(n_adapt, rank_dim, f_width),
        down_second_gradient.reshape(n_adapt, rank_dim, d_width),
    )


def solution(mesh):
    return jax.shard_map(
        on_device,
        mesh=mesh,
        in_specs=(
            P("row", "col"),
            P("row", "col"),
            P("col", "row"),
            P("col", "row"),
            P("col", "row"),
            P("col", "row"),
            P("row", "col"),
            P(None, None, "col"),
            P(None, None, "row"),
            P(None, None, "row"),
            P(None, None, "col"),
            P(),
            P(),
        ),
        out_specs=(
            P("row", "col"),
            P(None, None, "col"),
            P(None, None, "row"),
            P(None, None, "row"),
            P(None, None, "col"),
        ),
        check_vma=False,
    )
```

```python
import jax
import jax.numpy as jnp
from jax import lax
from jax.sharding import PartitionSpec as P

ADAPTER_SCALING = 2.0


def hot_rows(tenant, adapter, first_tok, tok_count, n_adapt, rank_dim):
    tok_ids = lax.dynamic_slice_in_dim(tenant, first_tok, tok_count)
    ten_hot = (tok_ids[:, None] == jnp.arange(adapter.shape[0], dtype=jnp.int32)[None, :]).astype(
        jnp.float32
    )
    ada_hot = (adapter[:, None] == jnp.arange(n_adapt, dtype=jnp.int32)[None, :]).astype(
        jnp.float32
    )
    return jnp.repeat(jnp.dot(ten_hot, ada_hot), rank_dim, axis=1)


def ring_gather(x, axis):
    n = lax.axis_size(axis)
    me = lax.axis_index(axis)
    out = jnp.zeros((n,) + x.shape, x.dtype)
    out = lax.dynamic_update_index_in_dim(out, x, me, 0)
    fwd = x
    bwd = x
    for step in range(1, n // 2 + 1):
        fwd = lax.ppermute(fwd, axis, [(i, (i + 1) % n) for i in range(n)])
        out = lax.dynamic_update_index_in_dim(out, fwd, (me - step) % n, 0)
        if step < n - step:
            bwd = lax.ppermute(bwd, axis, [(i, (i - 1) % n) for i in range(n)])
            out = lax.dynamic_update_index_in_dim(out, bwd, (me + step) % n, 0)
    return out.reshape((n * x.shape[0],) + x.shape[1:])


def on_device(
    inputs,
    cotangent,
    gate_pre,
    up_pre,
    w_gate,
    w_up,
    w_down,
    up_a,
    up_b,
    down_a,
    down_b,
    tenant,
    adapter,
):
    n_adapt, rank_dim, d_width = up_a.shape
    f_width = up_b.shape[2]
    arv = n_adapt * rank_dim
    tok_row = inputs.shape[0]
    tok_all = tenant.shape[0]
    tok_col = tok_all // lax.axis_size("col")
    up_a_all = up_a.reshape(arv, d_width)
    up_b_all = up_b.reshape(arv, f_width)
    down_a_all = down_a.reshape(arv, f_width)
    down_b_all = down_b.reshape(arv, d_width)
    token_row_mask = hot_rows(
        tenant, adapter, lax.axis_index("row") * tok_row, tok_row, n_adapt, rank_dim
    )
    z_part = jnp.dot(inputs, up_a_all.T, preferred_element_type=jnp.float32)
    q_part = jnp.dot(cotangent, down_b_all.T, preferred_element_type=jnp.float32)
    narrow_own = jnp.concatenate([z_part, q_part], axis=1).astype(jnp.bfloat16)
    packed_1 = jnp.concatenate([cotangent, inputs, narrow_own], axis=1)
    gathered_1 = lax.all_gather(packed_1, "row", axis=0, tiled=True)
    ct_column = gathered_1[:, :d_width]
    in_column = gathered_1[:, d_width : 2 * d_width]
    narrow_column = gathered_1[:, 2 * d_width :]
    dh_term = jnp.dot(ct_column, w_down.T, preferred_element_type=jnp.float32)
    summed_1 = lax.psum_scatter(
        jnp.concatenate([dh_term, narrow_column.astype(jnp.float32)], axis=1),
        "col",
        scatter_dimension=0,
        tiled=True,
    )
    dh_base = summed_1[:, :f_width]
    reduced_first_factor = summed_1[:, f_width:]
    active_tenant_mask = hot_rows(
        tenant, adapter, lax.axis_index("col") * tok_col, tok_col, n_adapt, rank_dim
    )
    up_adapter_output = (reduced_first_factor[:, :arv] * active_tenant_mask).astype(jnp.bfloat16)
    down_latent_rows = (
        ADAPTER_SCALING * reduced_first_factor[:, arv:] * active_tenant_mask
    ).astype(jnp.bfloat16)
    d_hidden = dh_base + jnp.dot(down_latent_rows, down_a_all, preferred_element_type=jnp.float32)
    gate_f = gate_pre.astype(jnp.float32)
    up_f = up_pre.astype(jnp.float32)
    sigma = jax.nn.sigmoid(gate_f)
    silu_g = gate_f * sigma
    hidden = (silu_g * up_f).astype(jnp.bfloat16)
    up_gradient_rows = (d_hidden * silu_g).astype(jnp.bfloat16)
    d_gate = (d_hidden * up_f * sigma * (1.0 + gate_f * (1.0 - sigma))).astype(jnp.bfloat16)
    z_hidden = jnp.dot(hidden, down_a_all.T, preferred_element_type=jnp.float32).astype(
        jnp.bfloat16
    )
    q_hidden = jnp.dot(up_gradient_rows, up_b_all.T, preferred_element_type=jnp.float32).astype(
        jnp.bfloat16
    )
    grad_down_a = jnp.dot(down_latent_rows.T, hidden, preferred_element_type=jnp.float32)
    up_second_gradient = ADAPTER_SCALING * jnp.dot(
        up_adapter_output.T, up_gradient_rows, preferred_element_type=jnp.float32
    )
    gathered_2 = ring_gather(
        jnp.concatenate([d_gate, up_gradient_rows, z_hidden, q_hidden], axis=1), "col"
    )
    (grad_down_a, up_second_gradient), gathered_2 = lax.optimization_barrier(
        ((grad_down_a, up_second_gradient), gathered_2)
    )
    grad_down_a, up_second_gradient = lax.psum((grad_down_a, up_second_gradient), "col")
    gate_rows = gathered_2[:, :f_width]
    up_rows = gathered_2[:, f_width : 2 * f_width]
    n_row = lax.axis_size("row")
    swapped_n = lax.all_to_all(gathered_2[:, 2 * f_width :], "row", 0, 0, tiled=True)
    reduced_second_factor = (
        swapped_n.reshape(n_row, tok_row, 2 * arv).astype(jnp.float32).sum(0)
    )
    down_adapter_output = (reduced_second_factor[:, :arv] * token_row_mask).astype(jnp.bfloat16)
    up_latent_rows = (
        ADAPTER_SCALING * reduced_second_factor[:, arv:] * token_row_mask
    ).astype(jnp.bfloat16)
    latent_own = jnp.concatenate([down_adapter_output, up_latent_rows], axis=1)
    latent_all = lax.all_to_all(jnp.tile(latent_own, (n_row, 1)), "row", 0, 0, tiled=True)
    grad_up_a = jnp.dot(latent_all[:, arv:].T, in_column, preferred_element_type=jnp.float32)
    down_second_gradient = ADAPTER_SCALING * jnp.dot(
        latent_all[:, :arv].T, ct_column, preferred_element_type=jnp.float32
    )
    dx_term = jnp.dot(gate_rows, w_gate.T, preferred_element_type=jnp.float32)
    dx_term = dx_term + jnp.dot(up_rows, w_up.T, preferred_element_type=jnp.float32)
    swapped_2 = lax.all_to_all(dx_term.astype(jnp.bfloat16), "row", 0, 0, tiled=True)
    dx_base = swapped_2.reshape(n_row, tok_row, d_width).astype(jnp.float32).sum(0)
    grad_inputs = (
        dx_base + jnp.dot(up_latent_rows, up_a_all, preferred_element_type=jnp.float32)
    ).astype(jnp.bfloat16)
    return (
        grad_inputs,
        grad_up_a.reshape(n_adapt, rank_dim, d_width),
        up_second_gradient.reshape(n_adapt, rank_dim, f_width),
        grad_down_a.reshape(n_adapt, rank_dim, f_width),
        down_second_gradient.reshape(n_adapt, rank_dim, d_width),
    )


def solution(mesh):
    return jax.shard_map(
        on_device,
        mesh=mesh,
        in_specs=(
            P("row", "col"),
            P("row", "col"),
            P("col", "row"),
            P("col", "row"),
            P("col", "row"),
            P("col", "row"),
            P("row", "col"),
            P(None, None, "col"),
            P(None, None, "row"),
            P(None, None, "row"),
            P(None, None, "col"),
            P(),
            P(),
        ),
        out_specs=(
            P("row", "col"),
            P(None, None, "col"),
            P(None, None, "row"),
            P(None, None, "row"),
            P(None, None, "col"),
        ),
        check_vma=False,
    )
```

```python
import jax
import jax.numpy as jnp
from jax import lax
from jax.sharding import PartitionSpec as P

ADAPTER_SCALING = 2.0


def hot_rows(tenant, adapter, first_tok, tok_count, n_adapt, rank_dim):
    tok_ids = lax.dynamic_slice_in_dim(tenant, first_tok, tok_count)
    ten_hot = (tok_ids[:, None] == jnp.arange(adapter.shape[0], dtype=jnp.int32)[None, :]).astype(
        jnp.float32
    )
    ada_hot = (adapter[:, None] == jnp.arange(n_adapt, dtype=jnp.int32)[None, :]).astype(
        jnp.float32
    )
    return jnp.repeat(jnp.dot(ten_hot, ada_hot), rank_dim, axis=1)


def on_device(
    inputs,
    cotangent,
    gate_pre,
    up_pre,
    w_gate,
    w_up,
    w_down,
    up_a,
    up_b,
    down_a,
    down_b,
    tenant,
    adapter,
):
    n_adapt, rank_dim, d_width = up_a.shape
    f_width = up_b.shape[2]
    arv = n_adapt * rank_dim
    tok_row = inputs.shape[0]
    tok_all = tenant.shape[0]
    tok_col = tok_all // lax.axis_size("col")
    up_a_all = up_a.reshape(arv, d_width)
    up_b_all = up_b.reshape(arv, f_width)
    down_a_all = down_a.reshape(arv, f_width)
    down_b_all = down_b.reshape(arv, d_width)
    token_row_mask = hot_rows(
        tenant, adapter, lax.axis_index("row") * tok_row, tok_row, n_adapt, rank_dim
    )
    z_part = jnp.dot(inputs, up_a_all.T, preferred_element_type=jnp.float32)
    q_part = jnp.dot(cotangent, down_b_all.T, preferred_element_type=jnp.float32)
    narrow_own = jnp.concatenate([z_part, q_part], axis=1).astype(jnp.bfloat16)
    packed_1 = jnp.concatenate([cotangent, narrow_own], axis=1)
    gathered_1 = lax.all_gather(packed_1, "row", axis=0, tiled=True)
    ct_column = gathered_1[:, :d_width]
    narrow_column = gathered_1[:, d_width:]
    inputs_tiled, gathered_1 = lax.optimization_barrier(
        (jnp.tile(inputs, (lax.axis_size("row"), 1)), gathered_1)
    )
    in_column = lax.all_to_all(inputs_tiled, "row", 0, 0, tiled=True)
    dh_term = jnp.dot(ct_column, w_down.T, preferred_element_type=jnp.float32)
    summed_1 = lax.psum_scatter(
        jnp.concatenate([dh_term, narrow_column.astype(jnp.float32)], axis=1),
        "col",
        scatter_dimension=0,
        tiled=True,
    )
    dh_base = summed_1[:, :f_width]
    reduced_first_factor = summed_1[:, f_width:]
    active_tenant_mask = hot_rows(
        tenant, adapter, lax.axis_index("col") * tok_col, tok_col, n_adapt, rank_dim
    )
    up_adapter_output = (reduced_first_factor[:, :arv] * active_tenant_mask).astype(jnp.bfloat16)
    down_latent_rows = (
        ADAPTER_SCALING * reduced_first_factor[:, arv:] * active_tenant_mask
    ).astype(jnp.bfloat16)
    d_hidden = dh_base + jnp.dot(down_latent_rows, down_a_all, preferred_element_type=jnp.float32)
    gate_f = gate_pre.astype(jnp.float32)
    up_f = up_pre.astype(jnp.float32)
    sigma = jax.nn.sigmoid(gate_f)
    silu_g = gate_f * sigma
    hidden = (silu_g * up_f).astype(jnp.bfloat16)
    up_gradient_rows = (d_hidden * silu_g).astype(jnp.bfloat16)
    d_gate = (d_hidden * up_f * sigma * (1.0 + gate_f * (1.0 - sigma))).astype(jnp.bfloat16)
    z_hidden = jnp.dot(hidden, down_a_all.T, preferred_element_type=jnp.float32).astype(
        jnp.bfloat16
    )
    q_hidden = jnp.dot(up_gradient_rows, up_b_all.T, preferred_element_type=jnp.float32).astype(
        jnp.bfloat16
    )
    grad_down_a = jnp.dot(down_latent_rows.T, hidden, preferred_element_type=jnp.float32)
    up_second_gradient = ADAPTER_SCALING * jnp.dot(
        up_adapter_output.T, up_gradient_rows, preferred_element_type=jnp.float32
    )
    packed_2, in_column = lax.optimization_barrier(
        (jnp.concatenate([d_gate, up_gradient_rows, z_hidden, q_hidden], axis=1), in_column)
    )
    gathered_2 = lax.all_gather(
        packed_2,
        "col",
        axis=0,
        tiled=True,
    )
    (grad_down_a, up_second_gradient), gathered_2 = lax.optimization_barrier(
        ((grad_down_a, up_second_gradient), gathered_2)
    )
    grad_down_a, up_second_gradient = lax.psum((grad_down_a, up_second_gradient), "col")
    gate_rows = gathered_2[:, :f_width]
    up_rows = gathered_2[:, f_width : 2 * f_width]
    n_row = lax.axis_size("row")
    swapped_n = lax.all_to_all(gathered_2[:, 2 * f_width :], "row", 0, 0, tiled=True)
    reduced_second_factor = (
        swapped_n.reshape(n_row, tok_row, 2 * arv).astype(jnp.float32).sum(0)
    )
    down_adapter_output = (reduced_second_factor[:, :arv] * token_row_mask).astype(jnp.bfloat16)
    up_latent_rows = (
        ADAPTER_SCALING * reduced_second_factor[:, arv:] * token_row_mask
    ).astype(jnp.bfloat16)
    latent_own = jnp.concatenate([down_adapter_output, up_latent_rows], axis=1)
    latent_all = lax.all_to_all(jnp.tile(latent_own, (n_row, 1)), "row", 0, 0, tiled=True)
    grad_up_a = jnp.dot(latent_all[:, arv:].T, in_column, preferred_element_type=jnp.float32)
    down_second_gradient = ADAPTER_SCALING * jnp.dot(
        latent_all[:, :arv].T, ct_column, preferred_element_type=jnp.float32
    )
    dx_term = jnp.dot(gate_rows, w_gate.T, preferred_element_type=jnp.float32)
    dx_term = dx_term + jnp.dot(up_rows, w_up.T, preferred_element_type=jnp.float32)
    swapped_2 = lax.all_to_all(dx_term.astype(jnp.bfloat16), "row", 0, 0, tiled=True)
    dx_base = swapped_2.reshape(n_row, tok_row, d_width).astype(jnp.float32).sum(0)
    grad_inputs = (
        dx_base + jnp.dot(up_latent_rows, up_a_all, preferred_element_type=jnp.float32)
    ).astype(jnp.bfloat16)
    return (
        grad_inputs,
        grad_up_a.reshape(n_adapt, rank_dim, d_width),
        up_second_gradient.reshape(n_adapt, rank_dim, f_width),
        grad_down_a.reshape(n_adapt, rank_dim, f_width),
        down_second_gradient.reshape(n_adapt, rank_dim, d_width),
    )


def solution(mesh):
    return jax.shard_map(
        on_device,
        mesh=mesh,
        in_specs=(
            P("row", "col"),
            P("row", "col"),
            P("col", "row"),
            P("col", "row"),
            P("col", "row"),
            P("col", "row"),
            P("row", "col"),
            P(None, None, "col"),
            P(None, None, "row"),
            P(None, None, "row"),
            P(None, None, "col"),
            P(),
            P(),
        ),
        out_specs=(
            P("row", "col"),
            P(None, None, "col"),
            P(None, None, "row"),
            P(None, None, "row"),
            P(None, None, "col"),
        ),
        check_vma=False,
    )
```

```python
import jax
import jax.numpy as jnp
from jax import lax
from jax.sharding import PartitionSpec as P

ADAPTER_SCALING = 2.0


def hot_rows(tenant, adapter, first_tok, tok_count, n_adapt, rank_dim):
    tok_ids = lax.dynamic_slice_in_dim(tenant, first_tok, tok_count)
    ten_hot = (tok_ids[:, None] == jnp.arange(adapter.shape[0], dtype=jnp.int32)[None, :]).astype(
        jnp.float32
    )
    ada_hot = (adapter[:, None] == jnp.arange(n_adapt, dtype=jnp.int32)[None, :]).astype(
        jnp.float32
    )
    return jnp.repeat(jnp.dot(ten_hot, ada_hot), rank_dim, axis=1)


def on_device(
    inputs,
    cotangent,
    gate_pre,
    up_pre,
    w_gate,
    w_up,
    w_down,
    up_a,
    up_b,
    down_a,
    down_b,
    tenant,
    adapter,
):
    n_adapt, rank_dim, d_width = up_a.shape
    f_width = up_b.shape[2]
    arv = n_adapt * rank_dim
    tok_row = inputs.shape[0]
    tok_all = tenant.shape[0]
    tok_col = tok_all // lax.axis_size("col")
    up_a_all = up_a.reshape(arv, d_width)
    up_b_all = up_b.reshape(arv, f_width)
    down_a_all = down_a.reshape(arv, f_width)
    down_b_all = down_b.reshape(arv, d_width)
    token_row_mask = hot_rows(
        tenant, adapter, lax.axis_index("row") * tok_row, tok_row, n_adapt, rank_dim
    )
    z_part = jnp.dot(inputs, up_a_all.T, preferred_element_type=jnp.float32)
    q_part = jnp.dot(cotangent, down_b_all.T, preferred_element_type=jnp.float32)
    narrow_own = jnp.concatenate([z_part, q_part], axis=1).astype(jnp.bfloat16)
    packed_1 = jnp.concatenate([cotangent, narrow_own], axis=1)
    gathered_1 = lax.all_gather(packed_1, "row", axis=0, tiled=True)
    ct_column = gathered_1[:, :d_width]
    narrow_column = gathered_1[:, d_width:]
    inputs_tiled, gathered_1 = lax.optimization_barrier(
        (jnp.tile(inputs, (lax.axis_size("row"), 1)), gathered_1)
    )
    in_column = lax.all_to_all(inputs_tiled, "row", 0, 0, tiled=True)
    dh_term = jnp.dot(ct_column, w_down.T, preferred_element_type=jnp.float32)
    summed_1 = lax.psum_scatter(
        jnp.concatenate([dh_term, narrow_column.astype(jnp.float32)], axis=1),
        "col",
        scatter_dimension=0,
        tiled=True,
    )
    dh_base = summed_1[:, :f_width]
    reduced_first_factor = summed_1[:, f_width:]
    active_tenant_mask = hot_rows(
        tenant, adapter, lax.axis_index("col") * tok_col, tok_col, n_adapt, rank_dim
    )
    up_adapter_output = (reduced_first_factor[:, :arv] * active_tenant_mask).astype(jnp.bfloat16)
    down_latent_rows = (
        ADAPTER_SCALING * reduced_first_factor[:, arv:] * active_tenant_mask
    ).astype(jnp.bfloat16)
    d_hidden = dh_base + jnp.dot(down_latent_rows, down_a_all, preferred_element_type=jnp.float32)
    gate_f = gate_pre.astype(jnp.float32)
    up_f = up_pre.astype(jnp.float32)
    sigma = jax.nn.sigmoid(gate_f)
    silu_g = gate_f * sigma
    hidden = (silu_g * up_f).astype(jnp.bfloat16)
    up_gradient_rows = (d_hidden * silu_g).astype(jnp.bfloat16)
    d_gate = (d_hidden * up_f * sigma * (1.0 + gate_f * (1.0 - sigma))).astype(jnp.bfloat16)
    z_hidden = jnp.dot(hidden, down_a_all.T, preferred_element_type=jnp.float32).astype(
        jnp.bfloat16
    )
    q_hidden = jnp.dot(up_gradient_rows, up_b_all.T, preferred_element_type=jnp.float32).astype(
        jnp.bfloat16
    )
    grad_down_a = jnp.dot(down_latent_rows.T, hidden, preferred_element_type=jnp.float32)
    up_second_gradient = ADAPTER_SCALING * jnp.dot(
        up_adapter_output.T, up_gradient_rows, preferred_element_type=jnp.float32
    )
    gathered_2 = lax.all_gather(
        jnp.concatenate([d_gate, up_gradient_rows, z_hidden, q_hidden], axis=1),
        "col",
        axis=0,
        tiled=True,
    )
    (grad_down_a, up_second_gradient), gathered_2, in_column = lax.optimization_barrier(
        ((grad_down_a, up_second_gradient), gathered_2, in_column)
    )
    grad_down_a, up_second_gradient = lax.psum((grad_down_a, up_second_gradient), "col")
    gate_rows = gathered_2[:, :f_width]
    up_rows = gathered_2[:, f_width : 2 * f_width]
    n_row = lax.axis_size("row")
    swapped_n = lax.all_to_all(gathered_2[:, 2 * f_width :], "row", 0, 0, tiled=True)
    reduced_second_factor = (
        swapped_n.reshape(n_row, tok_row, 2 * arv).astype(jnp.float32).sum(0)
    )
    down_adapter_output = (reduced_second_factor[:, :arv] * token_row_mask).astype(jnp.bfloat16)
    up_latent_rows = (
        ADAPTER_SCALING * reduced_second_factor[:, arv:] * token_row_mask
    ).astype(jnp.bfloat16)
    latent_own = jnp.concatenate([down_adapter_output, up_latent_rows], axis=1)
    latent_all = lax.all_to_all(jnp.tile(latent_own, (n_row, 1)), "row", 0, 0, tiled=True)
    grad_up_a = jnp.dot(latent_all[:, arv:].T, in_column, preferred_element_type=jnp.float32)
    down_second_gradient = ADAPTER_SCALING * jnp.dot(
        latent_all[:, :arv].T, ct_column, preferred_element_type=jnp.float32
    )
    dx_term = jnp.dot(gate_rows, w_gate.T, preferred_element_type=jnp.float32)
    dx_term = dx_term + jnp.dot(up_rows, w_up.T, preferred_element_type=jnp.float32)
    swapped_2 = lax.all_to_all(dx_term.astype(jnp.bfloat16), "row", 0, 0, tiled=True)
    dx_base = swapped_2.reshape(n_row, tok_row, d_width).astype(jnp.float32).sum(0)
    grad_inputs = (
        dx_base + jnp.dot(up_latent_rows, up_a_all, preferred_element_type=jnp.float32)
    ).astype(jnp.bfloat16)
    return (
        grad_inputs,
        grad_up_a.reshape(n_adapt, rank_dim, d_width),
        up_second_gradient.reshape(n_adapt, rank_dim, f_width),
        grad_down_a.reshape(n_adapt, rank_dim, f_width),
        down_second_gradient.reshape(n_adapt, rank_dim, d_width),
    )


def solution(mesh):
    return jax.shard_map(
        on_device,
        mesh=mesh,
        in_specs=(
            P("row", "col"),
            P("row", "col"),
            P("col", "row"),
            P("col", "row"),
            P("col", "row"),
            P("col", "row"),
            P("row", "col"),
            P(None, None, "col"),
            P(None, None, "row"),
            P(None, None, "row"),
            P(None, None, "col"),
            P(),
            P(),
        ),
        out_specs=(
            P("row", "col"),
            P(None, None, "col"),
            P(None, None, "row"),
            P(None, None, "row"),
            P(None, None, "col"),
        ),
        check_vma=False,
    )
```

```python
import jax
import jax.numpy as jnp
from jax import lax
from jax.sharding import PartitionSpec as P

ADAPTER_SCALING = 2.0


def hot_rows(tenant, adapter, first_tok, tok_count, n_adapt, rank_dim):
    tok_ids = lax.dynamic_slice_in_dim(tenant, first_tok, tok_count)
    ten_hot = (tok_ids[:, None] == jnp.arange(adapter.shape[0], dtype=jnp.int32)[None, :]).astype(
        jnp.float32
    )
    ada_hot = (adapter[:, None] == jnp.arange(n_adapt, dtype=jnp.int32)[None, :]).astype(
        jnp.float32
    )
    return jnp.repeat(jnp.dot(ten_hot, ada_hot), rank_dim, axis=1)


def on_device(
    inputs,
    cotangent,
    gate_pre,
    up_pre,
    w_gate,
    w_up,
    w_down,
    up_a,
    up_b,
    down_a,
    down_b,
    tenant,
    adapter,
):
    n_adapt, rank_dim, d_width = up_a.shape
    f_width = up_b.shape[2]
    arv = n_adapt * rank_dim
    tok_row = inputs.shape[0]
    tok_all = tenant.shape[0]
    tok_col = tok_all // lax.axis_size("col")
    up_a_all = up_a.reshape(arv, d_width)
    up_b_all = up_b.reshape(arv, f_width)
    down_a_all = down_a.reshape(arv, f_width)
    down_b_all = down_b.reshape(arv, d_width)
    token_row_mask = hot_rows(
        tenant, adapter, lax.axis_index("row") * tok_row, tok_row, n_adapt, rank_dim
    )
    z_part = jnp.dot(inputs, up_a_all.T, preferred_element_type=jnp.float32)
    q_part = jnp.dot(cotangent, down_b_all.T, preferred_element_type=jnp.float32)
    narrow_own = jnp.concatenate([z_part, q_part], axis=1).astype(jnp.bfloat16)
    packed_1 = jnp.concatenate([cotangent, narrow_own], axis=1)
    gathered_1 = lax.all_gather(packed_1, "row", axis=0, tiled=True)
    ct_column = gathered_1[:, :d_width]
    narrow_column = gathered_1[:, d_width:]
    inputs_tiled, gathered_1 = lax.optimization_barrier(
        (jnp.tile(inputs, (lax.axis_size("row"), 1)), gathered_1)
    )
    in_column = lax.all_to_all(inputs_tiled, "row", 0, 0, tiled=True)
    n_narrow = narrow_column.shape[1]
    w_ext = jnp.concatenate(
        [
            jnp.concatenate([w_down, jnp.zeros((f_width, n_narrow), w_down.dtype)], axis=1),
            jnp.concatenate(
                [jnp.zeros((n_narrow, d_width), w_down.dtype), jnp.eye(n_narrow, dtype=w_down.dtype)],
                axis=1,
            ),
        ],
        axis=0,
    )
    dh_ext = lax.dot_general(
        gathered_1, w_ext, (((1,), (1,)), ((), ())), preferred_element_type=jnp.float32
    )
    summed_1 = lax.psum_scatter(dh_ext, "col", scatter_dimension=0, tiled=True)
    dh_base = summed_1[:, :f_width]
    reduced_first_factor = summed_1[:, f_width:]
    active_tenant_mask = hot_rows(
        tenant, adapter, lax.axis_index("col") * tok_col, tok_col, n_adapt, rank_dim
    )
    up_adapter_output = (reduced_first_factor[:, :arv] * active_tenant_mask).astype(jnp.bfloat16)
    down_latent_rows = (
        ADAPTER_SCALING * reduced_first_factor[:, arv:] * active_tenant_mask
    ).astype(jnp.bfloat16)
    d_hidden = dh_base + jnp.dot(down_latent_rows, down_a_all, preferred_element_type=jnp.float32)
    gate_f = gate_pre.astype(jnp.float32)
    up_f = up_pre.astype(jnp.float32)
    sigma = jax.nn.sigmoid(gate_f)
    silu_g = gate_f * sigma
    hidden = (silu_g * up_f).astype(jnp.bfloat16)
    up_gradient_rows = (d_hidden * silu_g).astype(jnp.bfloat16)
    d_gate = (d_hidden * up_f * sigma * (1.0 + gate_f * (1.0 - sigma))).astype(jnp.bfloat16)
    z_hidden = jnp.dot(hidden, down_a_all.T, preferred_element_type=jnp.float32).astype(
        jnp.bfloat16
    )
    q_hidden = jnp.dot(up_gradient_rows, up_b_all.T, preferred_element_type=jnp.float32).astype(
        jnp.bfloat16
    )
    grad_down_a = jnp.dot(down_latent_rows.T, hidden, preferred_element_type=jnp.float32)
    up_second_gradient = ADAPTER_SCALING * jnp.dot(
        up_adapter_output.T, up_gradient_rows, preferred_element_type=jnp.float32
    )
    gathered_2 = lax.all_gather(
        jnp.concatenate([d_gate, up_gradient_rows, z_hidden, q_hidden], axis=1),
        "col",
        axis=0,
        tiled=True,
    )
    (grad_down_a, up_second_gradient), gathered_2, in_column = lax.optimization_barrier(
        ((grad_down_a, up_second_gradient), gathered_2, in_column)
    )
    grad_down_a, up_second_gradient = lax.psum((grad_down_a, up_second_gradient), "col")
    gate_rows = gathered_2[:, :f_width]
    up_rows = gathered_2[:, f_width : 2 * f_width]
    n_row = lax.axis_size("row")
    swapped_n = lax.all_to_all(gathered_2[:, 2 * f_width :], "row", 0, 0, tiled=True)
    reduced_second_factor = (
        swapped_n.reshape(n_row, tok_row, 2 * arv).astype(jnp.float32).sum(0)
    )
    down_adapter_output = (reduced_second_factor[:, :arv] * token_row_mask).astype(jnp.bfloat16)
    up_latent_rows = (
        ADAPTER_SCALING * reduced_second_factor[:, arv:] * token_row_mask
    ).astype(jnp.bfloat16)
    latent_own = jnp.concatenate([down_adapter_output, up_latent_rows], axis=1)
    latent_all = lax.all_to_all(jnp.tile(latent_own, (n_row, 1)), "row", 0, 0, tiled=True)
    grad_up_a = jnp.dot(latent_all[:, arv:].T, in_column, preferred_element_type=jnp.float32)
    down_second_gradient = ADAPTER_SCALING * jnp.dot(
        latent_all[:, :arv].T, ct_column, preferred_element_type=jnp.float32
    )
    dx_term = jnp.dot(gate_rows, w_gate.T, preferred_element_type=jnp.float32)
    dx_term = dx_term + jnp.dot(up_rows, w_up.T, preferred_element_type=jnp.float32)
    swapped_2 = lax.all_to_all(dx_term.astype(jnp.bfloat16), "row", 0, 0, tiled=True)
    dx_base = swapped_2.reshape(n_row, tok_row, d_width).astype(jnp.float32).sum(0)
    grad_inputs = (
        dx_base + jnp.dot(up_latent_rows, up_a_all, preferred_element_type=jnp.float32)
    ).astype(jnp.bfloat16)
    return (
        grad_inputs,
        grad_up_a.reshape(n_adapt, rank_dim, d_width),
        up_second_gradient.reshape(n_adapt, rank_dim, f_width),
        grad_down_a.reshape(n_adapt, rank_dim, f_width),
        down_second_gradient.reshape(n_adapt, rank_dim, d_width),
    )


def solution(mesh):
    return jax.shard_map(
        on_device,
        mesh=mesh,
        in_specs=(
            P("row", "col"),
            P("row", "col"),
            P("col", "row"),
            P("col", "row"),
            P("col", "row"),
            P("col", "row"),
            P("row", "col"),
            P(None, None, "col"),
            P(None, None, "row"),
            P(None, None, "row"),
            P(None, None, "col"),
            P(),
            P(),
        ),
        out_specs=(
            P("row", "col"),
            P(None, None, "col"),
            P(None, None, "row"),
            P(None, None, "row"),
            P(None, None, "col"),
        ),
        check_vma=False,
    )
```

```python
import jax
import jax.numpy as jnp
from jax import lax
from jax.sharding import PartitionSpec as P

ADAPTER_SCALING = 2.0


def hot_rows(tenant, adapter, first_tok, tok_count, n_adapt, rank_dim):
    tok_ids = lax.dynamic_slice_in_dim(tenant, first_tok, tok_count)
    ten_hot = (tok_ids[:, None] == jnp.arange(adapter.shape[0], dtype=jnp.int32)[None, :]).astype(
        jnp.float32
    )
    ada_hot = (adapter[:, None] == jnp.arange(n_adapt, dtype=jnp.int32)[None, :]).astype(
        jnp.float32
    )
    return jnp.repeat(jnp.dot(ten_hot, ada_hot), rank_dim, axis=1)


def on_device(
    inputs,
    cotangent,
    gate_pre,
    up_pre,
    w_gate,
    w_up,
    w_down,
    up_a,
    up_b,
    down_a,
    down_b,
    tenant,
    adapter,
):
    n_adapt, rank_dim, d_width = up_a.shape
    f_width = up_b.shape[2]
    arv = n_adapt * rank_dim
    tok_row = inputs.shape[0]
    tok_all = tenant.shape[0]
    tok_col = tok_all // lax.axis_size("col")
    up_a_all = up_a.reshape(arv, d_width)
    up_b_all = up_b.reshape(arv, f_width)
    down_a_all = down_a.reshape(arv, f_width)
    down_b_all = down_b.reshape(arv, d_width)
    token_row_mask = hot_rows(
        tenant, adapter, lax.axis_index("row") * tok_row, tok_row, n_adapt, rank_dim
    )
    z_part = jnp.dot(inputs, up_a_all.T, preferred_element_type=jnp.float32)
    q_part = jnp.dot(cotangent, down_b_all.T, preferred_element_type=jnp.float32)
    narrow_own = jnp.concatenate([z_part, q_part], axis=1).astype(jnp.bfloat16)
    packed_1 = jnp.concatenate([cotangent, narrow_own], axis=1)
    gathered_1 = lax.all_gather(packed_1, "row", axis=0, tiled=True)
    ct_column = gathered_1[:, :d_width]
    narrow_column = gathered_1[:, d_width:]
    inputs_tiled, gathered_1 = lax.optimization_barrier(
        (jnp.tile(inputs, (lax.axis_size("row"), 1)), gathered_1)
    )
    in_column = lax.all_to_all(inputs_tiled, "row", 0, 0, tiled=True)
    n_narrow = narrow_column.shape[1]
    w_ext = jnp.concatenate(
        [
            jnp.concatenate([w_down, jnp.zeros((f_width, n_narrow), w_down.dtype)], axis=1),
            jnp.concatenate(
                [jnp.zeros((n_narrow, d_width), w_down.dtype), jnp.eye(n_narrow, dtype=w_down.dtype)],
                axis=1,
            ),
        ],
        axis=0,
    )
    dh_ext = lax.dot_general(
        gathered_1, w_ext, (((1,), (1,)), ((), ())), preferred_element_type=jnp.float32
    )
    summed_1 = lax.psum_scatter(dh_ext, "col", scatter_dimension=0, tiled=True)
    dh_base = summed_1[:, :f_width]
    reduced_first_factor = summed_1[:, f_width:]
    active_tenant_mask = hot_rows(
        tenant, adapter, lax.axis_index("col") * tok_col, tok_col, n_adapt, rank_dim
    )
    up_adapter_output = (reduced_first_factor[:, :arv] * active_tenant_mask).astype(jnp.bfloat16)
    down_latent_rows = (
        ADAPTER_SCALING * reduced_first_factor[:, arv:] * active_tenant_mask
    ).astype(jnp.bfloat16)
    d_hidden = dh_base + jnp.dot(down_latent_rows, down_a_all, preferred_element_type=jnp.float32)
    gate_f = gate_pre.astype(jnp.float32)
    up_f = up_pre.astype(jnp.float32)
    sigma = jax.nn.sigmoid(gate_f)
    silu_g = gate_f * sigma
    hidden = (silu_g * up_f).astype(jnp.bfloat16)
    up_gradient_rows = (d_hidden * silu_g).astype(jnp.bfloat16)
    d_gate = (d_hidden * up_f * sigma * (1.0 + gate_f * (1.0 - sigma))).astype(jnp.bfloat16)
    z_hidden = jnp.dot(hidden, down_a_all.T, preferred_element_type=jnp.float32).astype(
        jnp.bfloat16
    )
    q_hidden = jnp.dot(up_gradient_rows, up_b_all.T, preferred_element_type=jnp.float32).astype(
        jnp.bfloat16
    )
    grad_down_a = jnp.dot(down_latent_rows.T, hidden, preferred_element_type=jnp.float32)
    up_second_gradient = ADAPTER_SCALING * jnp.dot(
        up_adapter_output.T, up_gradient_rows, preferred_element_type=jnp.float32
    )
    gathered_2 = lax.all_gather(
        jnp.concatenate([d_gate, up_gradient_rows, z_hidden, q_hidden], axis=1),
        "col",
        axis=0,
        tiled=True,
    )
    (grad_down_a, up_second_gradient), gathered_2, in_column = lax.optimization_barrier(
        ((grad_down_a, up_second_gradient), gathered_2, in_column)
    )
    grad_down_a, up_second_gradient = lax.psum((grad_down_a, up_second_gradient), "col")
    gate_rows = gathered_2[:, :f_width]
    up_rows = gathered_2[:, f_width : 2 * f_width]
    n_row = lax.axis_size("row")
    swapped_n = lax.all_to_all(gathered_2[:, 2 * f_width :], "row", 0, 0, tiled=True)
    reduced_second_factor = (
        swapped_n.reshape(n_row, tok_row, 2 * arv).astype(jnp.float32).sum(0)
    )
    down_adapter_output = (reduced_second_factor[:, :arv] * token_row_mask).astype(jnp.bfloat16)
    up_latent_rows = (
        ADAPTER_SCALING * reduced_second_factor[:, arv:] * token_row_mask
    ).astype(jnp.bfloat16)
    latent_own = jnp.concatenate([down_adapter_output, up_latent_rows], axis=1)
    latent_all = lax.all_to_all(jnp.tile(latent_own, (n_row, 1)), "row", 0, 0, tiled=True)
    grad_up_a = jnp.dot(latent_all[:, arv:].T, in_column, preferred_element_type=jnp.float32)
    down_second_gradient = ADAPTER_SCALING * jnp.dot(
        latent_all[:, :arv].T, ct_column, preferred_element_type=jnp.float32
    )
    w_both = jnp.concatenate(
        [w_gate, w_up, jnp.zeros((d_width, 4 * rank_dim * n_adapt // 2), w_gate.dtype)], axis=1
    )
    dx_term = lax.dot_general(
        gathered_2, w_both, (((1,), (1,)), ((), ())), preferred_element_type=jnp.float32
    )
    swapped_2 = lax.all_to_all(dx_term.astype(jnp.bfloat16), "row", 0, 0, tiled=True)
    dx_base = swapped_2.reshape(n_row, tok_row, d_width).astype(jnp.float32).sum(0)
    grad_inputs = (
        dx_base + jnp.dot(up_latent_rows, up_a_all, preferred_element_type=jnp.float32)
    ).astype(jnp.bfloat16)
    return (
        grad_inputs,
        grad_up_a.reshape(n_adapt, rank_dim, d_width),
        up_second_gradient.reshape(n_adapt, rank_dim, f_width),
        grad_down_a.reshape(n_adapt, rank_dim, f_width),
        down_second_gradient.reshape(n_adapt, rank_dim, d_width),
    )


def solution(mesh):
    return jax.shard_map(
        on_device,
        mesh=mesh,
        in_specs=(
            P("row", "col"),
            P("row", "col"),
            P("col", "row"),
            P("col", "row"),
            P("col", "row"),
            P("col", "row"),
            P("row", "col"),
            P(None, None, "col"),
            P(None, None, "row"),
            P(None, None, "row"),
            P(None, None, "col"),
            P(),
            P(),
        ),
        out_specs=(
            P("row", "col"),
            P(None, None, "col"),
            P(None, None, "row"),
            P(None, None, "row"),
            P(None, None, "col"),
        ),
        check_vma=False,
    )
```
